256 devices in a mesh: samp: 32 (over x, z), snp: 8 (over y, core).
Axes of the slice: x: 4, y: 4, z: 8, core: 2. Of those that a mesh axis runs over, the one named last changes fastest.
Arguments:
- dosages: float32 [49152, 8192], P('samp', 'snp'), as said below
- band_counts: int32 [16], P('snp'), may hold values from 1 to 4, as said below
Outputs:
- corr_tiles: float32 [512, 16, 4, 512], P('samp', 'snp')
The draws below stay inside these ranges and needn't reach their ends.
Inputs may be any that keep to these rules, and one draw needn't show every extreme that they name: b + band_counts[b] <= 16 for every block b, and the counts of all blocks sum to exactly 32. `dosages`: finite real values.
All inputs are finite; a program needn't handle non-finite values.
Results may differ from the reference program's by a relative error of at most 0.0001.
Values sent between devices are 32-bit elements; how exact they have to be, the bound alone decides.
No kernel may reach another device: no remote copies, remote signals or barrier semaphores. Data moves between devices by JAX's collectives and lax.ppermute only.
A program may use at most 192 MiB of HBM per device.

```python
import math
import jax
import jax.numpy as jnp
from jax import lax

BW = 512
BLK_DEV = 2
MAXBAND = 4
NB = 16
SNPS = 8192
SAMPLES = 49152
LIVE = 32


def draw_band_counts(key, part):
    key_heavy, key_rank = jax.random.split(jax.random.fold_in(key, 7))
    heavy_limit = (NB - BLK_DEV - MAXBAND + 1) // BLK_DEV
    heavy_device = jax.random.randint(key_heavy, (), 0, heavy_limit + 1)
    block_ids = jnp.arange(NB, dtype=jnp.int32)
    heavy_rows = block_ids // BLK_DEV == heavy_device
    eligible = jnp.logical_and(jnp.logical_not(heavy_rows), block_ids < NB - 1)
    scores = jax.random.randint(key_rank, (NB,), 0, 1 << 20) * NB + block_ids
    scores = jnp.where(eligible, scores, (1 << 20) * NB + NB + block_ids)
    ranking = jnp.argsort(jnp.argsort(scores))
    extra_count = LIVE - NB - BLK_DEV * (MAXBAND - 1)
    plus_one = jnp.logical_and(eligible, ranking < extra_count)
    result = 1 + jnp.where(heavy_rows, MAXBAND - 1, 0) + plus_one.astype(jnp.int32)
    return result.astype(jnp.int32)


def noise_field(key, shape):
    return jax.random.normal(key, shape, jnp.float32)


def draw_dosages(key, part):
    key_list = jax.random.split(jax.random.fold_in(key, 11), 7)
    position = (jnp.arange(SAMPLES, dtype=jnp.float32) / SAMPLES)[:, None]
    cline = 0.5 + position
    jitter = jnp.exp(jax.random.uniform(key_list[0], (SAMPLES, 1), jnp.float32, -0.6, 0.6))
    sample_scale = (1.0 + 2.0 * position) * jitter
    mix_weight = 0.35
    frequency = jnp.exp(jax.random.uniform(key_list[1], (1, SNPS), jnp.float32, math.log(0.05), math.log(0.5)))
    snp_scale = jnp.exp(jax.random.uniform(key_list[2], (1, SNPS), jnp.float32, math.log(0.15), math.log(1.5)))
    latent = noise_field(key_list[3], (SAMPLES, SNPS + 7))
    linked = jnp.zeros((SAMPLES, SNPS), jnp.float32)
    for window_pos in range(8):
        linked = linked + 0.35 * latent[:, window_pos:window_pos + SNPS]
    factors = jax.random.normal(key_list[4], (SAMPLES, 4), jnp.float32)
    loadings = jax.random.normal(key_list[5], (4, SNPS), jnp.float32)
    ancestry = jnp.zeros((SAMPLES, SNPS), jnp.float32)
    for factor_index in range(4):
        ancestry = ancestry + 0.5 * factors[:, factor_index:factor_index + 1] * loadings[factor_index:factor_index + 1, :]
    private = noise_field(key_list[6], (SAMPLES, SNPS))
    mixed = 0.6 * linked + mix_weight * ancestry + 0.6 * private
    return 2.0 * frequency * cline + snp_scale * sample_scale * mixed


def setup_inputs(seed: int = 0) -> dict:
    seeds = jax.random.split(jax.random.key(seed), 3)
    dosages = draw_dosages(jax.random.fold_in(seeds[2], 71), 0)
    band_counts = draw_band_counts(jax.random.fold_in(seeds[2], 71), 0)
    return dict(dosages=dosages, band_counts=band_counts)


def reference(dosages, band_counts):
    sample_total = dosages.shape[0]
    block_count = band_counts.shape[0]
    center = lax.optimization_barrier(jnp.sum(dosages, axis=0)) / sample_total
    deviation = dosages - center
    spread = lax.optimization_barrier(jnp.sum(deviation * deviation, axis=0)) / sample_total
    scaled = deviation / jnp.sqrt(spread + 1e-06)
    row_list = []
    for row_index in range(block_count):
        left_panel = scaled[:, row_index * BW:(row_index + 1) * BW]
        tile_list = []
        for band_index in range(MAXBAND):
            column_block = row_index + band_index
            if column_block < block_count:
                right_panel = scaled[:, column_block * BW:(column_block + 1) * BW]
                tile_value = lax.dot_general(left_panel, right_panel, (((0,), (0,)), ((), ())), precision=lax.Precision.HIGHEST, preferred_element_type=jnp.float32) / sample_total
                tile_value = jnp.where(band_index < band_counts[row_index], tile_value, jnp.zeros_like(tile_value))
            else:
                tile_value = jnp.zeros((BW, BW), dosages.dtype)
            tile_list.append(tile_value)
        row_list.append(jnp.stack(tile_list, axis=1))
    return jnp.stack(row_list, axis=1)
```

```python
import jax
import jax.numpy as jnp
from jax import lax
from jax.sharding import PartitionSpec as P

MAXBAND = 4


HIGHEST_MODE = lax.Precision.HIGHEST
epsilon_value = 1e-06
transposed_dims = (((0,), (0,)), ((), ()))


def shifted(value, axis, steps):
    count = lax.axis_size(axis)
    first, last = (max(0, -steps), min(count, count - steps))
    return lax.ppermute(value, axis, [(source, source + steps) for source in range(first, last)])


def slot_sum(local, index, count):
    slots = jnp.arange(count, dtype=jnp.int32)[:, None] == index
    return lax.psum(jnp.where(slots, local[None, :], 0.0), ("samp", "snp")).reshape(-1)


def on_device(dosages, band_counts):
    samp_rows, column_total = dosages.shape
    blocks_here = band_counts.shape[0]
    block_width = column_total // blocks_here
    band_limit = MAXBAND
    snp_count = lax.axis_size("snp")
    sample_total = samp_rows * lax.axis_size("samp")
    inverse_total = 1.0 / sample_total
    me = lax.axis_index("snp")

    reach = (band_limit - 1 + blocks_here - 1) // blocks_here
    raw_sources = [dosages]
    for offset in range(1, reach + 1):
        last_block = min(band_limit - 1 + blocks_here - 1, offset * blocks_here + blocks_here - 1)
        need = (last_block - offset * blocks_here + 1) * block_width
        raw_sources.append(shifted(dosages[:, :need], "snp", -offset))

    pad = reach * column_total
    column_sum = slot_sum(jnp.sum(dosages, axis=0), me, snp_count)
    center_all = jnp.concatenate([column_sum * inverse_total, jnp.zeros((max(pad, 0),), jnp.float32)])

    def center_of(offset, width):
        return lax.dynamic_slice_in_dim(center_all, (me + offset) * column_total, width)

    deviation = dosages - center_of(0, column_total)
    square_sum = slot_sum(jnp.sum(deviation * deviation, axis=0), me, snp_count)
    spread_all = jnp.concatenate([square_sum * inverse_total, jnp.ones((max(pad, 0),), jnp.float32)])
    inverse_all = 1.0 / jnp.sqrt(spread_all + epsilon_value)

    sources = [deviation]
    for offset in range(1, reach + 1):
        raw = raw_sources[offset]
        sources.append(raw - center_of(offset, raw.shape[1]))

    def tile(local_block, band_index):
        column_block = local_block + band_index
        source = sources[column_block // blocks_here]
        column_start = column_block % blocks_here * block_width
        left_panel = deviation[:, local_block * block_width : (local_block + 1) * block_width]
        right_panel = source[:, column_start : column_start + block_width]
        return lax.dot_general(
            left_panel,
            right_panel,
            transposed_dims,
            precision=HIGHEST_MODE,
            preferred_element_type=jnp.float32,
        )

    pairs = [(b, k) for b in range(blocks_here) for k in range(band_limit)]
    local_pairs = [(b, k) for (b, k) in pairs if b + k < blocks_here]
    remote_pairs = [(b, k) for (b, k) in pairs if b + k >= blocks_here]
    band_range = jnp.arange(band_limit, dtype=jnp.int32)
    live_mask = band_range[None, :] < band_counts[:, None]

    def reduced(chunk):
        terms = jnp.stack([jnp.where(live_mask[b, k], tile(b, k), 0.0) for (b, k) in chunk], axis=1)
        return lax.psum_scatter(terms, "samp", scatter_dimension=0, tiled=True)

    first = reduced(local_pairs)
    second = reduced(remote_pairs)
    placed = {}
    for index, pair in enumerate(local_pairs):
        placed[pair] = first[:, index]
    for index, pair in enumerate(remote_pairs):
        placed[pair] = second[:, index]

    own_rows = block_width // lax.axis_size("samp")
    row_start = lax.axis_index("samp") * own_rows
    row_list = []
    for local_block in range(blocks_here):
        row_scale = lax.dynamic_slice_in_dim(
            inverse_all, me * column_total + local_block * block_width + row_start, own_rows
        )
        band_list = []
        for band_index in range(band_limit):
            column_block = local_block + band_index
            column_scale = lax.dynamic_slice_in_dim(
                inverse_all, me * column_total + column_block * block_width, block_width
            )
            band_list.append(
                placed[(local_block, band_index)] * row_scale[:, None] * column_scale[None, :] * inverse_total
            )
        row_list.append(jnp.stack(band_list, axis=1))
    return jnp.stack(row_list, axis=1)


def solution(mesh):
    return jax.shard_map(
        on_device,
        mesh=mesh,
        in_specs=(P("samp", "snp"), P("snp")),
        out_specs=P("samp", "snp", None, None),
        check_vma=False,
    )
```

```python
import jax
import jax.numpy as jnp
from jax import lax
from jax.sharding import PartitionSpec as P

MAXBAND = 4


HIGHEST_MODE = lax.Precision.HIGHEST
epsilon_value = 1e-06
transposed_dims = (((0,), (0,)), ((), ()))


def shifted(value, axis, steps):
    count = lax.axis_size(axis)
    first, last = (max(0, -steps), min(count, count - steps))
    return lax.ppermute(value, axis, [(source, source + steps) for source in range(first, last)])


def on_device(dosages, band_counts):
    samp_rows, column_total = dosages.shape
    blocks_here = band_counts.shape[0]
    block_width = column_total // blocks_here
    band_limit = MAXBAND
    sample_total = samp_rows * lax.axis_size("samp")
    inverse_total = 1.0 / sample_total

    reach = (band_limit - 1 + blocks_here - 1) // blocks_here
    widths = [column_total]
    raw_sources = [dosages]
    for offset in range(1, reach + 1):
        last_block = min(band_limit - 1 + blocks_here - 1, offset * blocks_here + blocks_here - 1)
        need = (last_block - offset * blocks_here + 1) * block_width
        widths.append(need)
        raw_sources.append(shifted(dosages[:, :need], "snp", -offset))

    column_sum = lax.psum(jnp.sum(dosages, axis=0), "samp")
    center = column_sum * inverse_total
    deviation = dosages - center
    square_sum = lax.psum(jnp.sum(deviation * deviation, axis=0), "samp")
    spread = square_sum * inverse_total
    inverse_sd = 1.0 / jnp.sqrt(spread + epsilon_value)

    stats = jnp.stack([center, inverse_sd])
    scales = [inverse_sd]
    sources = [deviation]
    for offset in range(1, reach + 1):
        width = widths[offset]
        moved = shifted(stats[:, :width], "snp", -offset)
        scales.append(moved[1])
        sources.append(raw_sources[offset] - moved[0])

    def tile(local_block, band_index):
        column_block = local_block + band_index
        source = sources[column_block // blocks_here]
        column_start = column_block % blocks_here * block_width
        left_panel = deviation[:, local_block * block_width : (local_block + 1) * block_width]
        right_panel = source[:, column_start : column_start + block_width]
        return lax.dot_general(
            left_panel,
            right_panel,
            transposed_dims,
            precision=HIGHEST_MODE,
            preferred_element_type=jnp.float32,
        )

    band_range = jnp.arange(band_limit, dtype=jnp.int32)
    live_mask = band_range[None, :] < band_counts[:, None]
    row_list = []
    for local_block in range(blocks_here):
        band_list = [tile(local_block, band_index) for band_index in range(band_limit)]
        row_list.append(jnp.stack(band_list, axis=1))
    tile_term = jnp.stack(row_list, axis=1)
    reduced = lax.psum_scatter(
        jnp.where(live_mask[None, :, :, None], tile_term, 0.0),
        "samp",
        scatter_dimension=0,
        tiled=True,
    )

    own_rows = block_width // lax.axis_size("samp")
    row_start = lax.axis_index("samp") * own_rows
    row_list = []
    for local_block in range(blocks_here):
        row_scale = lax.dynamic_slice_in_dim(inverse_sd, local_block * block_width + row_start, own_rows)
        band_list = []
        for band_index in range(band_limit):
            column_block = local_block + band_index
            source_scale = scales[column_block // blocks_here]
            column_start = column_block % blocks_here * block_width
            column_scale = source_scale[column_start : column_start + block_width]
            band_list.append(
                reduced[:, local_block, band_index] * row_scale[:, None] * column_scale[None, :] * inverse_total
            )
        row_list.append(jnp.stack(band_list, axis=1))
    return jnp.stack(row_list, axis=1)


def solution(mesh):
    return jax.shard_map(
        on_device,
        mesh=mesh,
        in_specs=(P("samp", "snp"), P("snp")),
        out_specs=P("samp", "snp", None, None),
        check_vma=False,
    )
```

```python
import jax
import jax.numpy as jnp
from jax import lax
from jax.sharding import PartitionSpec as P

MAXBAND = 4


HIGHEST_MODE = lax.Precision.HIGH
epsilon_value = 1e-06
transposed_dims = (((0,), (0,)), ((), ()))


def shifted(value, axis, steps):
    count = lax.axis_size(axis)
    first, last = (max(0, -steps), min(count, count - steps))
    return lax.ppermute(value, axis, [(source, source + steps) for source in range(first, last)])


def on_device(dosages, band_counts):
    samp_rows, column_total = dosages.shape
    blocks_here = band_counts.shape[0]
    block_width = column_total // blocks_here
    band_limit = MAXBAND
    sample_total = samp_rows * lax.axis_size("samp")
    inverse_total = 1.0 / sample_total

    reach = (band_limit - 1 + blocks_here - 1) // blocks_here
    widths = [column_total]
    raw_sources = [dosages]
    for offset in range(1, reach + 1):
        last_block = min(band_limit - 1 + blocks_here - 1, offset * blocks_here + blocks_here - 1)
        need = (last_block - offset * blocks_here + 1) * block_width
        widths.append(need)
        raw_sources.append(shifted(dosages[:, :need], "snp", -offset))

    samp_count = lax.axis_size("samp")
    local_center = jnp.sum(dosages, axis=0) * (1.0 / samp_rows)
    local_deviation = dosages - local_center
    local_square = jnp.sum(local_deviation * local_deviation, axis=0)
    slots = jnp.arange(samp_count, dtype=jnp.int32)[:, None] == lax.axis_index("samp")
    gathered = lax.psum(
        jnp.concatenate([jnp.where(slots, local_center[None, :], 0.0), local_square[None, :]]), "samp"
    )
    slot_centers = gathered[:samp_count]
    center = jnp.sum(slot_centers, axis=0) * (1.0 / samp_count)
    offsets = slot_centers - center
    square_sum = gathered[samp_count] + samp_rows * jnp.sum(offsets * offsets, axis=0)
    deviation = dosages - center
    spread = square_sum * inverse_total
    inverse_sd = 1.0 / jnp.sqrt(spread + epsilon_value)

    stats = jnp.stack([center, inverse_sd])
    scales = [inverse_sd]
    sources = [deviation]
    for offset in range(1, reach + 1):
        width = widths[offset]
        moved = shifted(stats[:, :width], "snp", -offset)
        scales.append(moved[1])
        sources.append(raw_sources[offset] - moved[0])

    def tile(local_block, band_index):
        column_block = local_block + band_index
        source = sources[column_block // blocks_here]
        column_start = column_block % blocks_here * block_width
        left_panel = deviation[:, local_block * block_width : (local_block + 1) * block_width]
        right_panel = source[:, column_start : column_start + block_width]
        return lax.dot_general(
            left_panel,
            right_panel,
            transposed_dims,
            precision=HIGHEST_MODE,
            preferred_element_type=jnp.float32,
        )

    band_range = jnp.arange(band_limit, dtype=jnp.int32)
    live_mask = band_range[None, :] < band_counts[:, None]
    row_list = []
    for local_block in range(blocks_here):
        band_list = [tile(local_block, band_index) for band_index in range(band_limit)]
        row_list.append(jnp.stack(band_list, axis=1))
    tile_term = jnp.stack(row_list, axis=1)
    reduced = lax.psum_scatter(
        jnp.where(live_mask[None, :, :, None], tile_term, 0.0),
        "samp",
        scatter_dimension=0,
        tiled=True,
    )

    own_rows = block_width // lax.axis_size("samp")
    row_start = lax.axis_index("samp") * own_rows
    row_list = []
    for local_block in range(blocks_here):
        row_scale = lax.dynamic_slice_in_dim(inverse_sd, local_block * block_width + row_start, own_rows)
        band_list = []
        for band_index in range(band_limit):
            column_block = local_block + band_index
            source_scale = scales[column_block // blocks_here]
            column_start = column_block % blocks_here * block_width
            column_scale = source_scale[column_start : column_start + block_width]
            band_list.append(
                reduced[:, local_block, band_index] * row_scale[:, None] * column_scale[None, :] * inverse_total
            )
        row_list.append(jnp.stack(band_list, axis=1))
    return jnp.stack(row_list, axis=1)


def solution(mesh):
    return jax.shard_map(
        on_device,
        mesh=mesh,
        in_specs=(P("samp", "snp"), P("snp")),
        out_specs=P("samp", "snp", None, None),
        check_vma=False,
    )
```

```python
import jax
import jax.numpy as jnp
from jax import lax
from jax.sharding import PartitionSpec as P

MAXBAND = 4


HIGHEST_MODE = lax.Precision.HIGH
epsilon_value = 1e-06
transposed_dims = (((0,), (0,)), ((), ()))


def shifted(value, axis, steps):
    count = lax.axis_size(axis)
    first, last = (max(0, -steps), min(count, count - steps))
    return lax.ppermute(value, axis, [(source, source + steps) for source in range(first, last)])


def samp_size():
    return lax.axis_size("samp_x") * lax.axis_size("samp_z")


def samp_sum(value):
    return lax.psum(lax.psum(value, "samp_z"), "samp_x")


def on_device(dosages, band_counts):
    samp_rows, column_total = dosages.shape
    blocks_here = band_counts.shape[0]
    block_width = column_total // blocks_here
    band_limit = MAXBAND
    sample_total = samp_rows * samp_size()
    inverse_total = 1.0 / sample_total

    reach = (band_limit - 1 + blocks_here - 1) // blocks_here
    widths = [column_total]
    raw_sources = [dosages]
    for offset in range(1, reach + 1):
        last_block = min(band_limit - 1 + blocks_here - 1, offset * blocks_here + blocks_here - 1)
        need = (last_block - offset * blocks_here + 1) * block_width
        widths.append(need)
        raw_sources.append(shifted(dosages[:, :need], "snp", -offset))

    column_sum = samp_sum(jnp.sum(dosages, axis=0))
    center = column_sum * inverse_total
    deviation = dosages - center
    square_sum = samp_sum(jnp.sum(deviation * deviation, axis=0))
    spread = square_sum * inverse_total
    inverse_sd = 1.0 / jnp.sqrt(spread + epsilon_value)

    stats = jnp.stack([center, inverse_sd])
    scales = [inverse_sd]
    sources = [deviation]
    for offset in range(1, reach + 1):
        width = widths[offset]
        moved = shifted(stats[:, :width], "snp", -offset)
        scales.append(moved[1])
        sources.append(raw_sources[offset] - moved[0])

    def tile(local_block, band_index):
        column_block = local_block + band_index
        source = sources[column_block // blocks_here]
        column_start = column_block % blocks_here * block_width
        left_panel = deviation[:, local_block * block_width : (local_block + 1) * block_width]
        right_panel = source[:, column_start : column_start + block_width]
        return lax.dot_general(
            left_panel,
            right_panel,
            transposed_dims,
            precision=HIGHEST_MODE,
            preferred_element_type=jnp.float32,
        )

    band_range = jnp.arange(band_limit, dtype=jnp.int32)
    live_mask = band_range[None, :] < band_counts[:, None]
    row_list = []
    for local_block in range(blocks_here):
        band_list = [tile(local_block, band_index) for band_index in range(band_limit)]
        row_list.append(jnp.stack(band_list, axis=1))
    tile_term = jnp.stack(row_list, axis=1)
    reduced = lax.psum_scatter(
        jnp.where(live_mask[None, :, :, None], tile_term, 0.0),
        ("samp_x", "samp_z"),
        scatter_dimension=0,
        tiled=True,
    )

    own_rows = block_width // samp_size()
    row_start = (lax.axis_index("samp_x") * lax.axis_size("samp_z") + lax.axis_index("samp_z")) * own_rows
    row_list = []
    for local_block in range(blocks_here):
        row_scale = lax.dynamic_slice_in_dim(inverse_sd, local_block * block_width + row_start, own_rows)
        band_list = []
        for band_index in range(band_limit):
            column_block = local_block + band_index
            source_scale = scales[column_block // blocks_here]
            column_start = column_block % blocks_here * block_width
            column_scale = source_scale[column_start : column_start + block_width]
            band_list.append(
                reduced[:, local_block, band_index] * row_scale[:, None] * column_scale[None, :] * inverse_total
            )
        row_list.append(jnp.stack(band_list, axis=1))
    return jnp.stack(row_list, axis=1)


def solution(mesh):
    x_size = mesh.devices.shape[0] // 8 if mesh.devices.shape[0] % 8 == 0 else 1
    split = jax.sharding.Mesh(
        mesh.devices.reshape(x_size, mesh.devices.shape[0] // x_size, mesh.devices.shape[1]),
        ("samp_x", "samp_z", "snp"),
    )
    return jax.shard_map(
        on_device,
        mesh=split,
        in_specs=(P(("samp_x", "samp_z"), "snp"), P("snp")),
        out_specs=P(("samp_x", "samp_z"), "snp", None, None),
        check_vma=False,
    )
```

```python
import jax
import jax.numpy as jnp
from jax import lax
from jax.sharding import PartitionSpec as P

MAXBAND = 4


HIGHEST_MODE = lax.Precision.HIGH
epsilon_value = 1e-06
transposed_dims = (((0,), (0,)), ((), ()))


def shifted(value, axis, steps):
    count = lax.axis_size(axis)
    first, last = (max(0, -steps), min(count, count - steps))
    return lax.ppermute(value, axis, [(source, source + steps) for source in range(first, last)])


def ring_steps(chunks, axis, count):
    me = lax.axis_index(axis)
    half = chunks.shape[-1] // 2
    forward = [(i, (i + 1) % count) for i in range(count)]
    backward = [(i, (i - 1) % count) for i in range(count)]

    def own(index, part):
        piece = lax.dynamic_index_in_dim(chunks, index % count, 0, keepdims=False)
        return piece[..., :half] if part == 0 else piece[..., half:]

    up = own(me - 1 + count, 0)
    down = own(me + 1, 1)
    for step in range(count - 1):
        up = lax.ppermute(up, axis, forward) + own(me - step - 2 + 2 * count, 0)
        down = lax.ppermute(down, axis, backward) + own(me + step + 2, 1)
    return jnp.concatenate([up, down], axis=-1)


def ring_reduce_scatter(value, major, minor):
    major_count = lax.axis_size(major)
    minor_count = lax.axis_size(minor)
    rows = value.shape[0] // (major_count * minor_count)
    grouped = value.reshape((major_count, minor_count, rows) + value.shape[1:])
    by_minor = jnp.moveaxis(grouped, 1, 0)
    partial = ring_steps(by_minor, minor, minor_count)
    return ring_steps(partial, major, major_count)


def samp_size():
    return lax.axis_size("samp_x") * lax.axis_size("samp_z")


def samp_sum(value):
    return lax.psum(lax.psum(value, "samp_z"), "samp_x")


def on_device(dosages, band_counts):
    samp_rows, column_total = dosages.shape
    blocks_here = band_counts.shape[0]
    block_width = column_total // blocks_here
    band_limit = MAXBAND
    sample_total = samp_rows * samp_size()
    inverse_total = 1.0 / sample_total

    reach = (band_limit - 1 + blocks_here - 1) // blocks_here
    widths = [column_total]
    raw_sources = [dosages]
    for offset in range(1, reach + 1):
        last_block = min(band_limit - 1 + blocks_here - 1, offset * blocks_here + blocks_here - 1)
        need = (last_block - offset * blocks_here + 1) * block_width
        widths.append(need)
        raw_sources.append(shifted(dosages[:, :need], "snp", -offset))

    column_sum = samp_sum(jnp.sum(dosages, axis=0))
    center = column_sum * inverse_total
    deviation = dosages - center
    square_sum = samp_sum(jnp.sum(deviation * deviation, axis=0))
    spread = square_sum * inverse_total
    inverse_sd = 1.0 / jnp.sqrt(spread + epsilon_value)

    stats = jnp.stack([center, inverse_sd])
    scales = [inverse_sd]
    sources = [deviation]
    for offset in range(1, reach + 1):
        width = widths[offset]
        moved = shifted(stats[:, :width], "snp", -offset)
        scales.append(moved[1])
        sources.append(raw_sources[offset] - moved[0])

    def tile(local_block, band_index):
        column_block = local_block + band_index
        source = sources[column_block // blocks_here]
        column_start = column_block % blocks_here * block_width
        left_panel = deviation[:, local_block * block_width : (local_block + 1) * block_width]
        right_panel = source[:, column_start : column_start + block_width]
        return lax.dot_general(
            left_panel,
            right_panel,
            transposed_dims,
            precision=HIGHEST_MODE,
            preferred_element_type=jnp.float32,
        )

    band_range = jnp.arange(band_limit, dtype=jnp.int32)
    live_mask = band_range[None, :] < band_counts[:, None]
    row_list = []
    for local_block in range(blocks_here):
        band_list = [tile(local_block, band_index) for band_index in range(band_limit)]
        row_list.append(jnp.stack(band_list, axis=1))
    tile_term = jnp.stack(row_list, axis=1)
    reduced = ring_reduce_scatter(jnp.where(live_mask[None, :, :, None], tile_term, 0.0), "samp_x", "samp_z")

    own_rows = block_width // samp_size()
    row_start = (lax.axis_index("samp_x") * lax.axis_size("samp_z") + lax.axis_index("samp_z")) * own_rows
    row_list = []
    for local_block in range(blocks_here):
        row_scale = lax.dynamic_slice_in_dim(inverse_sd, local_block * block_width + row_start, own_rows)
        band_list = []
        for band_index in range(band_limit):
            column_block = local_block + band_index
            source_scale = scales[column_block // blocks_here]
            column_start = column_block % blocks_here * block_width
            column_scale = source_scale[column_start : column_start + block_width]
            band_list.append(
                reduced[:, local_block, band_index] * row_scale[:, None] * column_scale[None, :] * inverse_total
            )
        row_list.append(jnp.stack(band_list, axis=1))
    return jnp.stack(row_list, axis=1)


def solution(mesh):
    x_size = mesh.devices.shape[0] // 8 if mesh.devices.shape[0] % 8 == 0 else 1
    split = jax.sharding.Mesh(
        mesh.devices.reshape(x_size, mesh.devices.shape[0] // x_size, mesh.devices.shape[1]),
        ("samp_x", "samp_z", "snp"),
    )
    return jax.shard_map(
        on_device,
        mesh=split,
        in_specs=(P(("samp_x", "samp_z"), "snp"), P("snp")),
        out_specs=P(("samp_x", "samp_z"), "snp", None, None),
        check_vma=False,
    )
```

```python
import jax
import jax.numpy as jnp
from jax import lax
from jax.sharding import PartitionSpec as P

MAXBAND = 4


HIGHEST_MODE = lax.Precision.HIGH
epsilon_value = 1e-06
transposed_dims = (((0,), (0,)), ((), ()))


def shifted(value, axis, steps):
    count = lax.axis_size(axis)
    first, last = (max(0, -steps), min(count, count - steps))
    return lax.ppermute(value, axis, [(source, source + steps) for source in range(first, last)])


def ring_steps(chunks, axis, count):
    me = lax.axis_index(axis)
    half = chunks.shape[-1] // 2
    forward = [(i, (i + 1) % count) for i in range(count)]
    backward = [(i, (i - 1) % count) for i in range(count)]

    def own(index, part):
        piece = lax.dynamic_index_in_dim(chunks, index % count, 0, keepdims=False)
        return piece[..., :half] if part == 0 else piece[..., half:]

    up = own(me - 1 + count, 0)
    down = own(me + 1, 1)
    for step in range(count - 1):
        up, down = lax.optimization_barrier((up, down))
        up = lax.ppermute(up, axis, forward) + own(me - step - 2 + 2 * count, 0)
        down = lax.ppermute(down, axis, backward) + own(me + step + 2, 1)
    return jnp.concatenate([up, down], axis=-1)


def ring_reduce_scatter(value, major, minor):
    major_count = lax.axis_size(major)
    minor_count = lax.axis_size(minor)
    rows = value.shape[0] // (major_count * minor_count)
    grouped = value.reshape((major_count, minor_count, rows) + value.shape[1:])
    by_minor = jnp.moveaxis(grouped, 1, 0)
    partial = ring_steps(by_minor, minor, minor_count)
    return ring_steps(partial, major, major_count)


def samp_size():
    return lax.axis_size("samp_x") * lax.axis_size("samp_z")


def samp_sum(value):
    return lax.psum(lax.psum(value, "samp_z"), "samp_x")


def on_device(dosages, band_counts):
    samp_rows, column_total = dosages.shape
    blocks_here = band_counts.shape[0]
    block_width = column_total // blocks_here
    band_limit = MAXBAND
    sample_total = samp_rows * samp_size()
    inverse_total = 1.0 / sample_total

    reach = (band_limit - 1 + blocks_here - 1) // blocks_here
    widths = [column_total]
    raw_sources = [dosages]
    for offset in range(1, reach + 1):
        last_block = min(band_limit - 1 + blocks_here - 1, offset * blocks_here + blocks_here - 1)
        need = (last_block - offset * blocks_here + 1) * block_width
        widths.append(need)
        raw_sources.append(shifted(dosages[:, :need], "snp", -offset))

    column_sum = samp_sum(jnp.sum(dosages, axis=0))
    center = column_sum * inverse_total
    deviation = dosages - center
    square_sum = samp_sum(jnp.sum(deviation * deviation, axis=0))
    spread = square_sum * inverse_total
    inverse_sd = 1.0 / jnp.sqrt(spread + epsilon_value)

    stats = jnp.stack([center, inverse_sd])
    scales = [inverse_sd]
    sources = [deviation]
    for offset in range(1, reach + 1):
        width = widths[offset]
        moved = shifted(stats[:, :width], "snp", -offset)
        scales.append(moved[1])
        sources.append(raw_sources[offset] - moved[0])

    def tile(local_block, band_index):
        column_block = local_block + band_index
        source = sources[column_block // blocks_here]
        column_start = column_block % blocks_here * block_width
        left_panel = deviation[:, local_block * block_width : (local_block + 1) * block_width]
        right_panel = source[:, column_start : column_start + block_width]
        return lax.dot_general(
            left_panel,
            right_panel,
            transposed_dims,
            precision=HIGHEST_MODE,
            preferred_element_type=jnp.float32,
        )

    band_range = jnp.arange(band_limit, dtype=jnp.int32)
    live_mask = band_range[None, :] < band_counts[:, None]
    row_list = []
    for local_block in range(blocks_here):
        band_list = [tile(local_block, band_index) for band_index in range(band_limit)]
        row_list.append(jnp.stack(band_list, axis=1))
    tile_term = jnp.stack(row_list, axis=1)
    reduced = ring_reduce_scatter(jnp.where(live_mask[None, :, :, None], tile_term, 0.0), "samp_x", "samp_z")

    own_rows = block_width // samp_size()
    row_start = (lax.axis_index("samp_x") * lax.axis_size("samp_z") + lax.axis_index("samp_z")) * own_rows
    row_list = []
    for local_block in range(blocks_here):
        row_scale = lax.dynamic_slice_in_dim(inverse_sd, local_block * block_width + row_start, own_rows)
        band_list = []
        for band_index in range(band_limit):
            column_block = local_block + band_index
            source_scale = scales[column_block // blocks_here]
            column_start = column_block % blocks_here * block_width
            column_scale = source_scale[column_start : column_start + block_width]
            band_list.append(
                reduced[:, local_block, band_index] * row_scale[:, None] * column_scale[None, :] * inverse_total
            )
        row_list.append(jnp.stack(band_list, axis=1))
    return jnp.stack(row_list, axis=1)


def solution(mesh):
    x_size = mesh.devices.shape[0] // 8 if mesh.devices.shape[0] % 8 == 0 else 1
    split = jax.sharding.Mesh(
        mesh.devices.reshape(x_size, mesh.devices.shape[0] // x_size, mesh.devices.shape[1]),
        ("samp_x", "samp_z", "snp"),
    )
    return jax.shard_map(
        on_device,
        mesh=split,
        in_specs=(P(("samp_x", "samp_z"), "snp"), P("snp")),
        out_specs=P(("samp_x", "samp_z"), "snp", None, None),
        check_vma=False,
    )
```

```python
import jax
import jax.numpy as jnp
from jax import lax
from jax.sharding import PartitionSpec as P

MAXBAND = 4


HIGHEST_MODE = lax.Precision.HIGH
epsilon_value = 1e-06
transposed_dims = (((0,), (0,)), ((), ()))


def shifted(value, axis, steps):
    count = lax.axis_size(axis)
    first, last = (max(0, -steps), min(count, count - steps))
    return lax.ppermute(value, axis, [(source, source + steps) for source in range(first, last)])


def ring_steps(chunks, axis, count, chunk_axis=0):
    me = lax.axis_index(axis)
    half = chunks.shape[-1] // 2
    forward = [(i, (i + 1) % count) for i in range(count)]
    backward = [(i, (i - 1) % count) for i in range(count)]

    def own(index, part):
        piece = lax.dynamic_index_in_dim(chunks, index % count, chunk_axis, keepdims=False)
        return piece[..., :half] if part == 0 else piece[..., half:]

    up = own(me - 1 + count, 0)
    down = own(me + 1, 1)
    for step in range(count - 1):
        up, down = lax.optimization_barrier((up, down))
        up = lax.ppermute(up, axis, forward) + own(me - step - 2 + 2 * count, 0)
        down = lax.ppermute(down, axis, backward) + own(me + step + 2, 1)
    return jnp.concatenate([up, down], axis=-1)


def ring_reduce_scatter(value, major, minor):
    major_count = lax.axis_size(major)
    minor_count = lax.axis_size(minor)
    rows = value.shape[0] // (major_count * minor_count)
    grouped = value.reshape((major_count, minor_count, rows) + value.shape[1:])
    partial = ring_steps(grouped, minor, minor_count, 1)
    return ring_steps(partial, major, major_count)


def samp_size():
    return lax.axis_size("samp_x") * lax.axis_size("samp_z")


def samp_sum(value):
    return lax.psum(lax.psum(value, "samp_z"), "samp_x")


def on_device(dosages, band_counts):
    samp_rows, column_total = dosages.shape
    blocks_here = band_counts.shape[0]
    block_width = column_total // blocks_here
    band_limit = MAXBAND
    sample_total = samp_rows * samp_size()
    inverse_total = 1.0 / sample_total

    reach = (band_limit - 1 + blocks_here - 1) // blocks_here
    widths = [column_total]
    raw_sources = [dosages]
    for offset in range(1, reach + 1):
        last_block = min(band_limit - 1 + blocks_here - 1, offset * blocks_here + blocks_here - 1)
        need = (last_block - offset * blocks_here + 1) * block_width
        widths.append(need)
    raw_sources.append(shifted(dosages[:, : widths[1]], "snp", -1))
    snp_count = lax.axis_size("snp")
    far = lax.ppermute(dosages[:, : widths[2]], "snp", [(j + 2, j) for j in range(1, snp_count - 2, 2)])
    near = lax.ppermute(raw_sources[1][:, : widths[2]], "snp", [(j + 1, j) for j in range(0, snp_count - 1, 2)])
    raw_sources.append(far + near)

    column_sum = samp_sum(jnp.sum(dosages, axis=0))
    center = column_sum * inverse_total
    deviation = dosages - center
    square_sum = samp_sum(jnp.sum(deviation * deviation, axis=0))
    spread = square_sum * inverse_total
    inverse_sd = 1.0 / jnp.sqrt(spread + epsilon_value)

    stats = jnp.stack([center, inverse_sd])
    scales = [inverse_sd]
    sources = [deviation]
    for offset in range(1, reach + 1):
        width = widths[offset]
        moved = shifted(stats[:, :width], "snp", -offset)
        scales.append(moved[1])
        sources.append(raw_sources[offset] - moved[0])

    def tile(local_block, band_index):
        column_block = local_block + band_index
        source = sources[column_block // blocks_here]
        column_start = column_block % blocks_here * block_width
        left_panel = deviation[:, local_block * block_width : (local_block + 1) * block_width]
        right_panel = source[:, column_start : column_start + block_width]
        return lax.dot_general(
            left_panel,
            right_panel,
            transposed_dims,
            precision=HIGHEST_MODE,
            preferred_element_type=jnp.float32,
        )

    band_range = jnp.arange(band_limit, dtype=jnp.int32)
    live_mask = band_range[None, :] < band_counts[:, None]
    row_list = []
    for local_block in range(blocks_here):
        band_list = [tile(local_block, band_index) for band_index in range(band_limit)]
        row_list.append(jnp.stack(band_list, axis=1))
    tile_term = jnp.stack(row_list, axis=1)
    reduced = ring_reduce_scatter(jnp.where(live_mask[None, :, :, None], tile_term, 0.0), "samp_x", "samp_z")

    own_rows = block_width // samp_size()
    row_start = (lax.axis_index("samp_x") * lax.axis_size("samp_z") + lax.axis_index("samp_z")) * own_rows
    row_list = []
    for local_block in range(blocks_here):
        row_scale = lax.dynamic_slice_in_dim(inverse_sd, local_block * block_width + row_start, own_rows)
        band_list = []
        for band_index in range(band_limit):
            column_block = local_block + band_index
            source_scale = scales[column_block // blocks_here]
            column_start = column_block % blocks_here * block_width
            column_scale = source_scale[column_start : column_start + block_width]
            band_list.append(
                reduced[:, local_block, band_index] * row_scale[:, None] * column_scale[None, :] * inverse_total
            )
        row_list.append(jnp.stack(band_list, axis=1))
    return jnp.stack(row_list, axis=1)


def solution(mesh):
    x_size = mesh.devices.shape[0] // 8 if mesh.devices.shape[0] % 8 == 0 else 1
    split = jax.sharding.Mesh(
        mesh.devices.reshape(x_size, mesh.devices.shape[0] // x_size, mesh.devices.shape[1]),
        ("samp_x", "samp_z", "snp"),
    )
    return jax.shard_map(
        on_device,
        mesh=split,
        in_specs=(P(("samp_x", "samp_z"), "snp"), P("snp")),
        out_specs=P(("samp_x", "samp_z"), "snp", None, None),
        check_vma=False,
    )
```

```python
import jax
import jax.numpy as jnp
from jax import lax
from jax.sharding import PartitionSpec as P

MAXBAND = 4


HIGHEST_MODE = lax.Precision.HIGH
epsilon_value = 1e-06
transposed_dims = (((0,), (0,)), ((), ()))


def shifted(value, axis, steps):
    count = lax.axis_size(axis)
    first, last = (max(0, -steps), min(count, count - steps))
    return lax.ppermute(value, axis, [(source, source + steps) for source in range(first, last)])


def ring_steps(piece_of, axis, count):
    me = lax.axis_index(axis)
    forward = [(i, (i + 1) % count) for i in range(count)]
    backward = [(i, (i - 1) % count) for i in range(count)]
    up = piece_of(me - 1 + count, 0)
    down = piece_of(me + 1, 1)
    for step in range(count - 1):
        up, down = lax.optimization_barrier((up, down))
        up = lax.ppermute(up, axis, forward) + piece_of(me - step - 2 + 2 * count, 0)
        down = lax.ppermute(down, axis, backward) + piece_of(me + step + 2, 1)
    return jnp.concatenate([up, down], axis=-1)


def ring_reduce_scatter(tiles, major, minor):
    major_count = lax.axis_size(major)
    minor_count = lax.axis_size(minor)
    rows = tiles[0].shape[0] // (major_count * minor_count)
    half = tiles[0].shape[-1] // 2
    grouped = [t.reshape((major_count, minor_count, rows) + t.shape[1:]) for t in tiles]

    def first_piece(index, part):
        pieces = [lax.dynamic_index_in_dim(g, index % minor_count, 1, keepdims=False) for g in grouped]
        pieces = [p[..., :half] if part == 0 else p[..., half:] for p in pieces]
        return jnp.stack(pieces, axis=2)

    partial = ring_steps(first_piece, minor, minor_count)

    def second_piece(index, part):
        piece = lax.dynamic_index_in_dim(partial, index % major_count, 0, keepdims=False)
        return piece[..., :half] if part == 0 else piece[..., half:]

    return ring_steps(second_piece, major, major_count)


def samp_size():
    return lax.axis_size("samp_x") * lax.axis_size("samp_z")


def samp_sum(value):
    return lax.psum(lax.psum(value, "samp_z"), "samp_x")


def on_device(dosages, band_counts):
    samp_rows, column_total = dosages.shape
    blocks_here = band_counts.shape[0]
    block_width = column_total // blocks_here
    band_limit = MAXBAND
    sample_total = samp_rows * samp_size()
    inverse_total = 1.0 / sample_total

    reach = (band_limit - 1 + blocks_here - 1) // blocks_here
    widths = [column_total]
    raw_sources = [dosages]
    for offset in range(1, reach + 1):
        last_block = min(band_limit - 1 + blocks_here - 1, offset * blocks_here + blocks_here - 1)
        need = (last_block - offset * blocks_here + 1) * block_width
        widths.append(need)
    raw_sources.append(shifted(dosages[:, : widths[1]], "snp", -1))
    snp_count = lax.axis_size("snp")
    far = lax.ppermute(dosages[:, : widths[2]], "snp", [(j + 2, j) for j in range(1, snp_count - 2, 2)])
    near = lax.ppermute(raw_sources[1][:, : widths[2]], "snp", [(j + 1, j) for j in range(0, snp_count - 1, 2)])
    raw_sources.append(far + near)

    column_sum = samp_sum(jnp.sum(dosages, axis=0))
    center = column_sum * inverse_total
    deviation = dosages - center
    square_sum = samp_sum(jnp.sum(deviation * deviation, axis=0))
    spread = square_sum * inverse_total
    inverse_sd = 1.0 / jnp.sqrt(spread + epsilon_value)

    stats = jnp.stack([center, inverse_sd])
    scales = [inverse_sd]
    sources = [deviation]
    for offset in range(1, reach + 1):
        width = widths[offset]
        moved = shifted(stats[:, :width], "snp", -offset)
        scales.append(moved[1])
        sources.append(raw_sources[offset] - moved[0])

    def tile(local_block, band_index):
        column_block = local_block + band_index
        source = sources[column_block // blocks_here]
        column_start = column_block % blocks_here * block_width
        left_panel = deviation[:, local_block * block_width : (local_block + 1) * block_width]
        right_panel = source[:, column_start : column_start + block_width]
        return lax.dot_general(
            left_panel,
            right_panel,
            transposed_dims,
            precision=HIGHEST_MODE,
            preferred_element_type=jnp.float32,
        )

    band_range = jnp.arange(band_limit, dtype=jnp.int32)
    live_mask = band_range[None, :] < band_counts[:, None]
    tiles = [tile(local_block, band_index) for local_block in range(blocks_here) for band_index in range(band_limit)]
    summed = ring_reduce_scatter(tiles, "samp_x", "samp_z")
    reduced = summed.reshape((summed.shape[0], blocks_here, band_limit, summed.shape[-1]))

    own_rows = block_width // samp_size()
    row_start = (lax.axis_index("samp_x") * lax.axis_size("samp_z") + lax.axis_index("samp_z")) * own_rows
    row_list = []
    for local_block in range(blocks_here):
        row_scale = lax.dynamic_slice_in_dim(inverse_sd, local_block * block_width + row_start, own_rows)
        band_list = []
        for band_index in range(band_limit):
            column_block = local_block + band_index
            source_scale = scales[column_block // blocks_here]
            column_start = column_block % blocks_here * block_width
            column_scale = source_scale[column_start : column_start + block_width]
            scaled_tile = reduced[:, local_block, band_index] * row_scale[:, None] * column_scale[None, :] * inverse_total
            band_list.append(jnp.where(live_mask[local_block, band_index], scaled_tile, 0.0))
        row_list.append(jnp.stack(band_list, axis=1))
    return jnp.stack(row_list, axis=1)


def solution(mesh):
    x_size = mesh.devices.shape[0] // 8 if mesh.devices.shape[0] % 8 == 0 else 1
    split = jax.sharding.Mesh(
        mesh.devices.reshape(x_size, mesh.devices.shape[0] // x_size, mesh.devices.shape[1]),
        ("samp_x", "samp_z", "snp"),
    )
    return jax.shard_map(
        on_device,
        mesh=split,
        in_specs=(P(("samp_x", "samp_z"), "snp"), P("snp")),
        out_specs=P(("samp_x", "samp_z"), "snp", None, None),
        check_vma=False,
    )
```

```python
import jax
import jax.numpy as jnp
from jax import lax
from jax.sharding import PartitionSpec as P

MAXBAND = 4


HIGHEST_MODE = lax.Precision.HIGH
epsilon_value = 1e-06
transposed_dims = (((0,), (0,)), ((), ()))


def shifted(value, axis, steps):
    count = lax.axis_size(axis)
    first, last = (max(0, -steps), min(count, count - steps))
    return lax.ppermute(value, axis, [(source, source + steps) for source in range(first, last)])


class Ring:
    def __init__(self, piece_of, axis, count):
        self.piece_of, self.axis, self.count = piece_of, axis, count
        self.me = lax.axis_index(axis)
        self.state = (piece_of(self.me - 1 + count, 0), piece_of(self.me + 1, 1))
        self.step = 0

    def advance(self):
        count, me = self.count, self.me
        up, down = self.state
        forward = [(i, (i + 1) % count) for i in range(count)]
        backward = [(i, (i - 1) % count) for i in range(count)]
        up = lax.ppermute(up, self.axis, forward) + self.piece_of(me - self.step - 2 + 2 * count, 0)
        down = lax.ppermute(down, self.axis, backward) + self.piece_of(me + self.step + 2, 1)
        self.state = (up, down)
        self.step += 1

    def done(self):
        return self.step == self.count - 1

    def result(self):
        return jnp.concatenate(self.state, axis=-1)


def run_together(rings):
    while not all(ring.done() for ring in rings):
        live = [ring for ring in rings if not ring.done()]
        states = lax.optimization_barrier(tuple(ring.state for ring in live))
        for ring, state in zip(live, states):
            ring.state = state
            ring.advance()
    return [ring.result() for ring in rings]


def sliced(piece, part, width):
    return piece[..., part * width : (part + 1) * width]


def ring_reduce_scatter(tiles, major, minor):
    major_count = lax.axis_size(major)
    minor_count = lax.axis_size(minor)
    rows = tiles[0].shape[0] // (major_count * minor_count)
    quarter = tiles[0].shape[-1] // 4
    grouped = [t.reshape((major_count, minor_count, rows) + t.shape[1:]) for t in tiles]

    def first_piece(axis_of_chunk, offset, count):
        def piece_of(index, part):
            pieces = [lax.dynamic_index_in_dim(g, index % count, axis_of_chunk, keepdims=False) for g in grouped]
            return jnp.stack([sliced(p, offset + part, quarter) for p in pieces], axis=2)

        return piece_of

    def second_piece(partial, count):
        def piece_of(index, part):
            piece = lax.dynamic_index_in_dim(partial, index % count, 0, keepdims=False)
            return sliced(piece, part, quarter)

        return piece_of

    early = run_together(
        [Ring(first_piece(1, 0, minor_count), minor, minor_count), Ring(first_piece(0, 2, major_count), major, major_count)]
    )
    late = run_together(
        [Ring(second_piece(early[0], major_count), major, major_count), Ring(second_piece(early[1], minor_count), minor, minor_count)]
    )
    return jnp.concatenate(late, axis=-1)


def samp_size():
    return lax.axis_size("samp_x") * lax.axis_size("samp_z")


def samp_sum(value):
    return lax.psum(lax.psum(value, "samp_z"), "samp_x")


def on_device(dosages, band_counts):
    samp_rows, column_total = dosages.shape
    blocks_here = band_counts.shape[0]
    block_width = column_total // blocks_here
    band_limit = MAXBAND
    sample_total = samp_rows * samp_size()
    inverse_total = 1.0 / sample_total

    reach = (band_limit - 1 + blocks_here - 1) // blocks_here
    widths = [column_total]
    raw_sources = [dosages]
    for offset in range(1, reach + 1):
        last_block = min(band_limit - 1 + blocks_here - 1, offset * blocks_here + blocks_here - 1)
        need = (last_block - offset * blocks_here + 1) * block_width
        widths.append(need)
    raw_sources.append(shifted(dosages[:, : widths[1]], "snp", -1))
    snp_count = lax.axis_size("snp")
    far = lax.ppermute(dosages[:, : widths[2]], "snp", [(j + 2, j) for j in range(1, snp_count - 2, 2)])
    near = lax.ppermute(raw_sources[1][:, : widths[2]], "snp", [(j + 1, j) for j in range(0, snp_count - 1, 2)])
    raw_sources.append(far + near)

    column_sum = samp_sum(jnp.sum(dosages, axis=0))
    center = column_sum * inverse_total
    deviation = dosages - center
    square_sum = samp_sum(jnp.sum(deviation * deviation, axis=0))
    spread = square_sum * inverse_total
    inverse_sd = 1.0 / jnp.sqrt(spread + epsilon_value)

    stats = jnp.stack([center, inverse_sd])
    scales = [inverse_sd]
    sources = [deviation]
    for offset in range(1, reach + 1):
        width = widths[offset]
        moved = shifted(stats[:, :width], "snp", -offset)
        scales.append(moved[1])
        sources.append(raw_sources[offset] - moved[0])

    def tile(local_block, band_index):
        column_block = local_block + band_index
        source = sources[column_block // blocks_here]
        column_start = column_block % blocks_here * block_width
        left_panel = deviation[:, local_block * block_width : (local_block + 1) * block_width]
        right_panel = source[:, column_start : column_start + block_width]
        return lax.dot_general(
            left_panel,
            right_panel,
            transposed_dims,
            precision=HIGHEST_MODE,
            preferred_element_type=jnp.float32,
        )

    band_range = jnp.arange(band_limit, dtype=jnp.int32)
    live_mask = band_range[None, :] < band_counts[:, None]
    tiles = [tile(local_block, band_index) for local_block in range(blocks_here) for band_index in range(band_limit)]
    summed = ring_reduce_scatter(tiles, "samp_x", "samp_z")
    reduced = summed.reshape((summed.shape[0], blocks_here, band_limit, summed.shape[-1]))

    own_rows = block_width // samp_size()
    row_start = (lax.axis_index("samp_x") * lax.axis_size("samp_z") + lax.axis_index("samp_z")) * own_rows
    row_list = []
    for local_block in range(blocks_here):
        row_scale = lax.dynamic_slice_in_dim(inverse_sd, local_block * block_width + row_start, own_rows)
        band_list = []
        for band_index in range(band_limit):
            column_block = local_block + band_index
            source_scale = scales[column_block // blocks_here]
            column_start = column_block % blocks_here * block_width
            column_scale = source_scale[column_start : column_start + block_width]
            scaled_tile = reduced[:, local_block, band_index] * row_scale[:, None] * column_scale[None, :] * inverse_total
            band_list.append(jnp.where(live_mask[local_block, band_index], scaled_tile, 0.0))
        row_list.append(jnp.stack(band_list, axis=1))
    return jnp.stack(row_list, axis=1)


def solution(mesh):
    x_size = mesh.devices.shape[0] // 8 if mesh.devices.shape[0] % 8 == 0 else 1
    split = jax.sharding.Mesh(
        mesh.devices.reshape(x_size, mesh.devices.shape[0] // x_size, mesh.devices.shape[1]),
        ("samp_x", "samp_z", "snp"),
    )
    return jax.shard_map(
        on_device,
        mesh=split,
        in_specs=(P(("samp_x", "samp_z"), "snp"), P("snp")),
        out_specs=P(("samp_x", "samp_z"), "snp", None, None),
        check_vma=False,
    )
```

```python
import jax
import jax.numpy as jnp
from jax import lax
from jax.sharding import PartitionSpec as P

MAXBAND = 4


HIGHEST_MODE = lax.Precision.HIGH
epsilon_value = 1e-06
transposed_dims = (((0,), (0,)), ((), ()))


def shifted(value, axis, steps):
    count = lax.axis_size(axis)
    first, last = (max(0, -steps), min(count, count - steps))
    return lax.ppermute(value, axis, [(source, source + steps) for source in range(first, last)])


def ring_steps(piece_of, axis, count):
    me = lax.axis_index(axis)
    forward = [(i, (i + 1) % count) for i in range(count)]
    backward = [(i, (i - 1) % count) for i in range(count)]

    def hop(step, carry):
        up, down = lax.optimization_barrier(carry)
        up = lax.ppermute(up, axis, forward) + piece_of(me - step - 2 + 2 * count, 0)
        down = lax.ppermute(down, axis, backward) + piece_of(me + step + 2, 1)
        return up, down

    up, down = lax.fori_loop(0, count - 1, hop, (piece_of(me - 1 + count, 0), piece_of(me + 1, 1)))
    return jnp.concatenate([up, down], axis=-1)


def ring_reduce_scatter(tiles, major, minor):
    major_count = lax.axis_size(major)
    minor_count = lax.axis_size(minor)
    rows = tiles[0].shape[0] // (major_count * minor_count)
    half = tiles[0].shape[-1] // 2
    grouped = [t.reshape((major_count, minor_count, rows) + t.shape[1:]) for t in tiles]

    def first_piece(index, part):
        pieces = [lax.dynamic_index_in_dim(g, index % minor_count, 1, keepdims=False) for g in grouped]
        pieces = [p[..., :half] if part == 0 else p[..., half:] for p in pieces]
        return jnp.stack(pieces, axis=2)

    partial = ring_steps(first_piece, minor, minor_count)

    def second_piece(index, part):
        piece = lax.dynamic_index_in_dim(partial, index % major_count, 0, keepdims=False)
        return piece[..., :half] if part == 0 else piece[..., half:]

    return ring_steps(second_piece, major, major_count)


def samp_size():
    return lax.axis_size("samp_x") * lax.axis_size("samp_z")


def samp_sum(value):
    return lax.psum(lax.psum(value, "samp_z"), "samp_x")


def on_device(dosages, band_counts):
    samp_rows, column_total = dosages.shape
    blocks_here = band_counts.shape[0]
    block_width = column_total // blocks_here
    band_limit = MAXBAND
    sample_total = samp_rows * samp_size()
    inverse_total = 1.0 / sample_total

    reach = (band_limit - 1 + blocks_here - 1) // blocks_here
    widths = [column_total]
    raw_sources = [dosages]
    for offset in range(1, reach + 1):
        last_block = min(band_limit - 1 + blocks_here - 1, offset * blocks_here + blocks_here - 1)
        need = (last_block - offset * blocks_here + 1) * block_width
        widths.append(need)
    raw_sources.append(shifted(dosages[:, : widths[1]], "snp", -1))
    snp_count = lax.axis_size("snp")
    far = lax.ppermute(dosages[:, : widths[2]], "snp", [(j + 2, j) for j in range(1, snp_count - 2, 2)])
    near = lax.ppermute(raw_sources[1][:, : widths[2]], "snp", [(j + 1, j) for j in range(0, snp_count - 1, 2)])
    raw_sources.append(far + near)

    column_sum = samp_sum(jnp.sum(dosages, axis=0))
    center = column_sum * inverse_total
    deviation = dosages - center
    square_sum = samp_sum(jnp.sum(deviation * deviation, axis=0))
    spread = square_sum * inverse_total
    inverse_sd = 1.0 / jnp.sqrt(spread + epsilon_value)

    stats = jnp.stack([center, inverse_sd])
    scales = [inverse_sd]
    sources = [deviation]
    for offset in range(1, reach + 1):
        width = widths[offset]
        moved = shifted(stats[:, :width], "snp", -offset)
        scales.append(moved[1])
        sources.append(raw_sources[offset] - moved[0])

    def tile(local_block, band_index):
        column_block = local_block + band_index
        source = sources[column_block // blocks_here]
        column_start = column_block % blocks_here * block_width
        left_panel = deviation[:, local_block * block_width : (local_block + 1) * block_width]
        right_panel = source[:, column_start : column_start + block_width]
        return lax.dot_general(
            left_panel,
            right_panel,
            transposed_dims,
            precision=HIGHEST_MODE,
            preferred_element_type=jnp.float32,
        )

    band_range = jnp.arange(band_limit, dtype=jnp.int32)
    live_mask = band_range[None, :] < band_counts[:, None]
    tiles = [tile(local_block, band_index) for local_block in range(blocks_here) for band_index in range(band_limit)]
    summed = ring_reduce_scatter(tiles, "samp_x", "samp_z")
    reduced = summed.reshape((summed.shape[0], blocks_here, band_limit, summed.shape[-1]))

    own_rows = block_width // samp_size()
    row_start = (lax.axis_index("samp_x") * lax.axis_size("samp_z") + lax.axis_index("samp_z")) * own_rows
    row_list = []
    for local_block in range(blocks_here):
        row_scale = lax.dynamic_slice_in_dim(inverse_sd, local_block * block_width + row_start, own_rows)
        band_list = []
        for band_index in range(band_limit):
            column_block = local_block + band_index
            source_scale = scales[column_block // blocks_here]
            column_start = column_block % blocks_here * block_width
            column_scale = source_scale[column_start : column_start + block_width]
            scaled_tile = reduced[:, local_block, band_index] * row_scale[:, None] * column_scale[None, :] * inverse_total
            band_list.append(jnp.where(live_mask[local_block, band_index], scaled_tile, 0.0))
        row_list.append(jnp.stack(band_list, axis=1))
    return jnp.stack(row_list, axis=1)


def solution(mesh):
    x_size = mesh.devices.shape[0] // 8 if mesh.devices.shape[0] % 8 == 0 else 1
    split = jax.sharding.Mesh(
        mesh.devices.reshape(x_size, mesh.devices.shape[0] // x_size, mesh.devices.shape[1]),
        ("samp_x", "samp_z", "snp"),
    )
    return jax.shard_map(
        on_device,
        mesh=split,
        in_specs=(P(("samp_x", "samp_z"), "snp"), P("snp")),
        out_specs=P(("samp_x", "samp_z"), "snp", None, None),
        check_vma=False,
    )
```
